128 devices in a mesh: pix: 8 (over y_hi, z), tm: 16 (over x, y_lo, core).
Axes of the slice: x: 4, y: 4 (y_hi: 2, y_lo: 2; y = y_hi * 2 + y_lo), z: 4, core: 2. Of those that a mesh axis runs over, the one named last changes fastest.
Arguments:
- frames: float32 [16, 192, 12288], P('tm', 'pix'), may hold values from 0.05 to 5
- pixel_order: int32 [12288], replicated, may hold values from 0 to 12287, each once
- cycle_sizes: int32 [64], replicated, may hold values from 1 to 384, 12288 in all
- kernel: float32 [5], replicated, may hold values from 0.1 to 1
Outputs:
- correlation: float32 [64, 3072, 3072], P('pix', 'tm')
The draws below stay inside these ranges and needn't reach their ends.
Inputs may be any that keep to these rules, and one draw needn't show every extreme that they name: `cycle_sizes`: every cycle has one or more pixels, the sizes sum to 12288, and one cycle has exactly 384.
All inputs are finite; a program needn't handle non-finite values.
Results may differ from the reference program's by a relative error of at most 0.00005.
Values sent between devices are 32-bit elements; how exact they have to be, the bound alone decides.
No kernel may reach another device: no remote copies, remote signals or barrier semaphores. Data moves between devices by JAX's collectives and lax.ppermute only.
A program may use at most 256 MiB of HBM per device.

```python
import math
import jax
import jax.numpy as jnp
import numpy as np
from jax import lax

CYCLES = 64
TBLK = 192
REACH = 2
PIXELS = 12288
FRAMES = 3072
CAP = 384


def level_of(own_key, shape, shards, smallest, high):
    def one(dim, shards_of):
        draws = jax.random.uniform(jax.random.fold_in(jax.random.fold_in(own_key, 6), dim), (shards_of,), jnp.float32, smallest / len(shards), high / len(shards))
        return jnp.repeat(jnp.exp(draws), shape[dim] // shards_of).reshape((-1,) + (1,) * (len(shape) - dim - 1))

    factor_of = one(*shards[0])
    for cut in shards[1:]:
        factor_of = factor_of * one(*cut)
    return factor_of


def split_up(number_of, total, reach, slope):
    loads = [(1 << 20) // math.isqrt(rank ** slope) + 1 for rank in range(2, number_of + 1)]
    rest, given = total - reach - (number_of - 1), [1] * (number_of - 1)
    while rest > 0:
        free = [i for i in range(number_of - 1) if given[i] < reach]
        pool, left = sum([loads[i] for i in free]), rest
        for i in free:
            extra = min(reach - given[i], max(1, left * loads[i] // pool), rest)
            given[i] = given[i] + extra
            rest = rest - extra
    return np.array([reach] + given)


def uneven(stream_key, number_of, total, limit, slope):
    if number_of == 2:
        one = jax.random.randint(stream_key, (), max(1, total - limit), min(limit, total - 1) + 1)
        return jnp.stack([one, total - one])
    tallies = jnp.asarray(split_up(number_of, total, limit, slope), jnp.int32)
    twos = (number_of - 1) // 2
    donor, receiver = tallies[1:1 + 2 * twos:2], tallies[2:2 + 2 * twos:2]
    margin = jnp.minimum(donor - 1, limit - receiver)
    passed = jax.random.randint(jax.random.fold_in(stream_key, 1), (twos,), 0, 1 << 20) % (margin + 1)
    tallies = tallies.at[1:1 + 2 * twos:2].set(donor - passed).at[2:2 + 2 * twos:2].set(receiver + passed)
    return tallies[jax.random.permutation(jax.random.fold_in(stream_key, 2), number_of)]


def setup_inputs(seed: int = 0) -> dict:
    key_list = jax.random.split(jax.random.key(seed), 5)
    return {
        "frames": jnp.clip(jnp.exp(math.log(5.0) - 4.6051702 * jax.random.uniform(key_list[0], (FRAMES // TBLK, TBLK, PIXELS), jnp.float32) ** level_of(key_list[0], (FRAMES // TBLK, TBLK, PIXELS), ((0, 16), (1, 8)), -0.2, 0.2)), 0.05, 5.0),
        "pixel_order": jax.random.permutation(key_list[1], PIXELS).astype(jnp.int32),
        "cycle_sizes": uneven(key_list[2], CYCLES, PIXELS, CAP, 2).astype(jnp.int32),
        "kernel": jnp.clip(jnp.exp(jax.random.uniform(key_list[3], (2 * REACH + 1,), jnp.float32, math.log(0.1), math.log(1.0))), 0.1, 1.0),
    }


def smooth_last(values, kernel):
    count = values.shape[-1]
    padded = jnp.pad(values, ((0, 0), (REACH, REACH)))
    result = kernel[0] * padded[:, 0:count]
    for shift_step in range(1, 2 * REACH + 1):
        result = result + kernel[shift_step] * padded[:, shift_step:shift_step + count]
    return result


def smooth_first(values, kernel):
    count = values.shape[0]
    padded = jnp.pad(values, ((REACH, REACH), (0, 0)))
    result = kernel[0] * padded[0:count]
    for shift_step in range(1, 2 * REACH + 1):
        result = result + kernel[shift_step] * padded[shift_step:shift_step + count]
    return result


def reference(frames, pixel_order, cycle_sizes, kernel):
    series = frames.reshape(FRAMES, PIXELS)
    starts = (jnp.cumsum(cycle_sizes) - cycle_sizes).astype(jnp.int32)
    slots = jnp.arange(CAP, dtype=jnp.int32)
    where_idx = jnp.minimum(starts[:, None] + slots[None, :], PIXELS - 1).astype(jnp.int32)
    valid = slots[None, :] < cycle_sizes[:, None]
    columns = pixel_order[where_idx]

    def one_cycle(packed):
        cols, mask, size = packed
        block = jnp.where(mask[None, :], series[:, cols], 0.0)
        total = jnp.sum(block, axis=1)
        product = jnp.dot(block, block.T, precision=lax.Precision.HIGHEST, preferred_element_type=jnp.float32)
        normed = product * size.astype(jnp.float32) / (total[:, None] * total[None, :])
        return smooth_first(smooth_last(normed, kernel), kernel)

    return lax.map(one_cycle, (columns, valid, cycle_sizes))
```

```python
import functools

import jax
import jax.numpy as jnp
from jax import lax
from jax.experimental import pallas as pl
from jax.experimental.pallas import tpu as pltpu
from jax.sharding import PartitionSpec as P

REACH = 2


def pick_kernel(owned, cap, first_ref, starts_ref, sizes_ref, order_ref, pixels_ref, out_ref):
    out_ref[...] = jnp.zeros_like(out_ref)
    first = first_ref[0]
    for r in range(owned):
        start = starts_ref[first + r]
        size = sizes_ref[first + r]

        def body(c, carry, r=r, start=start):
            row = order_ref[start + c]
            out_ref[pl.ds(r * cap + c, 1), :] = pixels_ref[pl.ds(row, 1), :]
            return carry

        lax.fori_loop(0, size, body, 0)


def pick(first, starts, sizes, order, pixels, owned, cap):
    count, width = pixels.shape
    smem = pl.BlockSpec(memory_space=pltpu.SMEM)
    vmem = pl.BlockSpec(memory_space=pltpu.VMEM)
    return pl.pallas_call(
        functools.partial(pick_kernel, owned, cap),
        out_shape=jax.ShapeDtypeStruct((owned * cap, width), pixels.dtype),
        in_specs=[smem, smem, smem, smem, vmem],
        out_specs=vmem,
        compiler_params=pltpu.CompilerParams(vmem_limit_bytes=40 * 1024 * 1024),
    )(first, starts, sizes, order, pixels)


def halo_frames(block, width):
    count = lax.axis_size("tm")
    forward = [(i, i + 1) for i in range(count - 1)]
    backward = [(i + 1, i) for i in range(count - 1)]
    n = block.shape[-1]
    low = lax.ppermute(block[..., n - width :], "tm", forward)
    high = lax.ppermute(block[..., :width], "tm", backward)
    return jnp.concatenate([low, block, high], axis=-1)


def per_device(frames, pixel_order, cycle_sizes, kernel):
    block = frames[0]
    cycles = cycle_sizes.shape[0]
    pixels = block.shape[1]
    cap = 2 * pixels // cycles
    owned = cycles // lax.axis_size("pix")
    starts = (jnp.cumsum(cycle_sizes) - cycle_sizes).astype(jnp.int32)
    first = (lax.axis_index("pix") * owned).astype(jnp.int32).reshape(1)

    series = lax.all_gather(block, "pix", axis=0, tiled=True)
    tblk = series.shape[0]
    picked = pick(first, starts, cycle_sizes, pixel_order, series.T, owned, cap)
    picked = picked.reshape(owned, cap, tblk)

    total = jnp.sum(picked, axis=1, keepdims=True)
    scaled = picked / total
    rimmed = halo_frames(scaled, REACH)
    smooth = kernel[0] * rimmed[..., 0:tblk]
    for shift_step in range(1, 2 * REACH + 1):
        smooth = smooth + kernel[shift_step] * rimmed[..., shift_step : shift_step + tblk]
    smooth = jnp.swapaxes(smooth, 1, 2)

    scale = lax.dynamic_slice_in_dim(cycle_sizes, first[0], owned).astype(jnp.float32)
    left = smooth * scale[:, None, None]
    right = lax.all_gather(smooth, "tm", axis=1, tiled=True)
    return jnp.einsum(
        "rfs,rgs->rfg",
        left,
        right,
        precision=lax.Precision.HIGH,
        preferred_element_type=jnp.float32,
    )


def solution(mesh):
    placed = (P("tm", "pix", None), P(), P(), P())
    return jax.shard_map(
        per_device, mesh=mesh, in_specs=placed, out_specs=P("pix", "tm", None), check_vma=False
    )
```

```python
import jax
import jax.numpy as jnp
from jax import lax
from jax.sharding import Mesh
from jax.sharding import PartitionSpec as P

REACH = 2
PIX = ("yh", "z")
TM = ("x", "yl", "c")
CHIPS = ("x", "yl")


def halo_frames(block, width):
    count = lax.axis_size(TM)
    forward = [(i, i + 1) for i in range(count - 1)]
    backward = [(i + 1, i) for i in range(count - 1)]
    n = block.shape[-1]
    low = lax.ppermute(block[..., n - width :], TM, forward)
    high = lax.ppermute(block[..., :width], TM, backward)
    return jnp.concatenate([low, block, high], axis=-1)


def correlate(left, right):
    return jnp.einsum(
        "rfs,rgs->rfg", left, right, precision=lax.Precision.HIGH, preferred_element_type=jnp.float32
    )


def per_device(frames, pixel_order, cycle_sizes, kernel):
    block = frames[0]
    sub, pixels = block.shape
    cycles = cycle_sizes.shape[0]
    cap = 2 * pixels // cycles
    groups = lax.axis_size(PIX)
    owned = cycles // groups
    half = owned // 2
    window = owned * cap
    starts = (jnp.cumsum(cycle_sizes) - cycle_sizes).astype(jnp.int32)
    me = lax.axis_index(PIX)

    ordered = jnp.take(block.T, pixel_order, axis=0)
    ordered = jnp.pad(ordered, ((0, window), (0, 0)))
    chunks = jnp.stack(
        [lax.dynamic_slice_in_dim(ordered, starts[d * owned], window, 0) for d in range(groups)]
    )
    got = lax.all_to_all(chunks, PIX, 0, 0, tiled=True)
    got = jnp.pad(got, ((0, 0), (0, cap), (0, 0)))

    base = starts[me * owned]
    slots = jnp.arange(cap, dtype=jnp.int32)
    picked = []
    for l in range(owned):
        r = me * owned + l
        rows = lax.dynamic_slice_in_dim(got, starts[r] - base, cap, 1)
        picked.append(jnp.where((slots < cycle_sizes[r])[None, :, None], rows, 0.0))
    picked = jnp.stack(picked)
    picked = jnp.transpose(picked, (0, 2, 1, 3)).reshape(owned, cap, groups * sub)
    tblk = groups * sub

    total = jnp.sum(picked, axis=1, keepdims=True)
    scaled = picked / total
    rimmed = halo_frames(scaled, REACH)
    smooth = kernel[0] * rimmed[..., 0:tblk]
    for shift_step in range(1, 2 * REACH + 1):
        smooth = smooth + kernel[shift_step] * rimmed[..., shift_step : shift_step + tblk]
    smooth = jnp.swapaxes(smooth, 1, 2)

    core = lax.axis_index("c")
    keep = lax.dynamic_slice_in_dim(smooth, core * half, half, 0)
    give = lax.dynamic_slice_in_dim(smooth, (1 - core) * half, half, 0)
    other = lax.ppermute(give, "c", [(0, 1), (1, 0)])
    pair = jnp.where(core == 0, jnp.concatenate([keep, other], 1), jnp.concatenate([other, keep], 1))
    right = lax.all_gather(pair, CHIPS, axis=1, tiled=True)

    scale = lax.dynamic_slice_in_dim(cycle_sizes, me * owned + core * half, half).astype(jnp.float32)
    scale = scale[:, None, None]
    sent = correlate(other * scale, right)
    back = lax.ppermute(sent, "c", [(0, 1), (1, 0)])
    mine = correlate(keep * scale, right)
    return jnp.where(core == 0, jnp.concatenate([mine, back], 0), jnp.concatenate([back, mine], 0))


def solution(mesh):
    pix, tm = mesh.shape["pix"], mesh.shape["tm"]
    fine = Mesh(mesh.devices.reshape(2, pix // 2, tm // 4, 2, 2), PIX + TM)
    placed = (P(TM, PIX, None), P(), P(), P())
    return jax.shard_map(
        per_device, mesh=fine, in_specs=placed, out_specs=P(PIX, TM, None), check_vma=False
    )
```

```python
import jax
import jax.numpy as jnp
from jax import lax
from jax.sharding import Mesh
from jax.sharding import PartitionSpec as P

REACH = 2
PIX = ("yh", "z")
TM = ("x", "yl", "c")
CHIPS = ("x", "yl")


def halo_frames(block, width):
    count = lax.axis_size(TM)
    forward = [(i, i + 1) for i in range(count - 1)]
    backward = [(i + 1, i) for i in range(count - 1)]
    n = block.shape[-1]
    low = lax.ppermute(block[..., n - width :], TM, forward)
    high = lax.ppermute(block[..., :width], TM, backward)
    return jnp.concatenate([low, block, high], axis=-1)


def correlate(left, right):
    return jnp.einsum(
        "rfs,rgs->rfg", left, right, precision=lax.Precision.HIGH, preferred_element_type=jnp.float32
    )


def per_device(frames, pixel_order, cycle_sizes, kernel):
    block = frames[0]
    sub, pixels = block.shape
    cycles = cycle_sizes.shape[0]
    cap = 2 * pixels // cycles
    groups = lax.axis_size(PIX)
    owned = cycles // groups
    half = owned // 2
    window = owned * cap
    starts = (jnp.cumsum(cycle_sizes) - cycle_sizes).astype(jnp.int32)
    me = lax.axis_index(PIX)

    ordered = jnp.take(block.T, pixel_order, axis=0)
    ordered = jnp.pad(ordered, ((0, window), (0, 0)))
    chunks = jnp.stack(
        [lax.dynamic_slice_in_dim(ordered, starts[d * owned], window, 0) for d in range(groups)]
    )
    got = lax.all_to_all(chunks, PIX, 0, 0, tiled=True)
    got = jnp.pad(got, ((0, 0), (0, cap), (0, 0)))

    base = starts[me * owned]
    slots = jnp.arange(cap, dtype=jnp.int32)
    picked = []
    for l in range(owned):
        r = me * owned + l
        rows = lax.dynamic_slice_in_dim(got, starts[r] - base, cap, 1)
        picked.append(jnp.where((slots < cycle_sizes[r])[None, :, None], rows, 0.0))
    picked = jnp.stack(picked)
    picked = jnp.transpose(picked, (0, 2, 1, 3)).reshape(owned, cap, groups * sub)
    tblk = groups * sub

    total = jnp.sum(picked, axis=1, keepdims=True)
    scaled = picked / total
    rimmed = halo_frames(scaled, REACH)
    smooth = kernel[0] * rimmed[..., 0:tblk]
    for shift_step in range(1, 2 * REACH + 1):
        smooth = smooth + kernel[shift_step] * rimmed[..., shift_step : shift_step + tblk]
    smooth = jnp.swapaxes(smooth, 1, 2)

    core = lax.axis_index("c")
    spots = lax.axis_size(TM)
    chunks = jnp.broadcast_to(smooth.reshape(1, 2, half, tblk, cap), (spots // 2, 2, half, tblk, cap))
    chunks = chunks.reshape(spots * half, tblk, cap)
    right = lax.all_to_all(chunks, TM, 0, 1, tiled=True)

    keep = lax.dynamic_slice_in_dim(smooth, core * half, half, 0)
    sibling = lax.axis_index(TM) + 1 - 2 * core
    other = lax.dynamic_slice_in_dim(right, sibling * tblk, tblk, 1)

    scale = lax.dynamic_slice_in_dim(cycle_sizes, me * owned + core * half, half).astype(jnp.float32)
    scale = scale[:, None, None]
    sent = correlate(other * scale, right)
    back = lax.ppermute(sent, "c", [(0, 1), (1, 0)])
    mine = correlate(keep * scale, right)
    return jnp.where(core == 0, jnp.concatenate([mine, back], 0), jnp.concatenate([back, mine], 0))


def solution(mesh):
    pix, tm = mesh.shape["pix"], mesh.shape["tm"]
    fine = Mesh(mesh.devices.reshape(2, pix // 2, tm // 4, 2, 2), PIX + TM)
    placed = (P(TM, PIX, None), P(), P(), P())
    return jax.shard_map(
        per_device, mesh=fine, in_specs=placed, out_specs=P(PIX, TM, None), check_vma=False
    )
```

```python
import jax
import jax.numpy as jnp
from jax import lax
from jax.sharding import PartitionSpec as P

REACH = 2
PARTS = 2


def halo_frames(block, width):
    count = lax.axis_size("tm")
    forward = [(i, i + 1) for i in range(count - 1)]
    backward = [(i + 1, i) for i in range(count - 1)]
    n = block.shape[-1]
    low = lax.ppermute(block[..., n - width :], "tm", forward)
    high = lax.ppermute(block[..., :width], "tm", backward)
    return jnp.concatenate([low, block, high], axis=-1)


def correlate(left, right):
    return jnp.einsum(
        "rfs,rgs->rfg", left, right, precision=lax.Precision.HIGH, preferred_element_type=jnp.float32
    )


def per_device(frames, pixel_order, cycle_sizes, kernel):
    block = frames[0]
    sub, pixels = block.shape
    cycles = cycle_sizes.shape[0]
    cap = 2 * pixels // cycles
    groups = lax.axis_size("pix")
    owned = cycles // groups
    step = owned // PARTS
    window = step * cap
    tblk = groups * sub
    starts = (jnp.cumsum(cycle_sizes) - cycle_sizes).astype(jnp.int32)
    me = lax.axis_index("pix")
    slots = jnp.arange(cap, dtype=jnp.int32)

    ordered = jnp.take(block.T, pixel_order, axis=0)
    ordered = jnp.pad(ordered, ((0, window), (0, 0)))

    outs = []
    for part in range(PARTS):
        chunks = jnp.stack(
            [
                lax.dynamic_slice_in_dim(ordered, starts[d * owned + part * step], window, 0)
                for d in range(groups)
            ]
        )
        got = lax.all_to_all(chunks, "pix", 0, 0, tiled=True)
        got = jnp.pad(got, ((0, 0), (0, cap), (0, 0)))
        first = me * owned + part * step
        picked = []
        for l in range(step):
            rows = lax.dynamic_slice_in_dim(got, starts[first + l] - starts[first], cap, 1)
            picked.append(jnp.where((slots < cycle_sizes[first + l])[None, :, None], rows, 0.0))
        picked = jnp.stack(picked)
        picked = jnp.transpose(picked, (0, 2, 1, 3)).reshape(step, cap, tblk)

        total = jnp.sum(picked, axis=1, keepdims=True)
        rimmed = halo_frames(picked / total, REACH)
        smooth = kernel[0] * rimmed[..., 0:tblk]
        for shift_step in range(1, 2 * REACH + 1):
            smooth = smooth + kernel[shift_step] * rimmed[..., shift_step : shift_step + tblk]
        smooth = jnp.swapaxes(smooth, 1, 2)

        scale = lax.dynamic_slice_in_dim(cycle_sizes, first, step).astype(jnp.float32)
        right = lax.all_gather(smooth, "tm", axis=1, tiled=True)
        outs.append(correlate(smooth * scale[:, None, None], right))
    return jnp.concatenate(outs, 0)


def solution(mesh):
    placed = (P("tm", "pix", None), P(), P(), P())
    return jax.shard_map(
        per_device, mesh=mesh, in_specs=placed, out_specs=P("pix", "tm", None), check_vma=False
    )
```

```python
import jax
import jax.numpy as jnp
from jax import lax
from jax.sharding import PartitionSpec as P

REACH = 2
PARTS = 4


def halo_frames(block, width):
    count = lax.axis_size("tm")
    forward = [(i, i + 1) for i in range(count - 1)]
    backward = [(i + 1, i) for i in range(count - 1)]
    n = block.shape[-1]
    low = lax.ppermute(block[..., n - width :], "tm", forward)
    high = lax.ppermute(block[..., :width], "tm", backward)
    return jnp.concatenate([low, block, high], axis=-1)


def correlate(left, right):
    return jnp.einsum(
        "rfs,rgs->rfg", left, right, precision=lax.Precision.HIGH, preferred_element_type=jnp.float32
    )


def per_device(frames, pixel_order, cycle_sizes, kernel):
    block = frames[0]
    sub, pixels = block.shape
    cycles = cycle_sizes.shape[0]
    cap = 2 * pixels // cycles
    groups = lax.axis_size("pix")
    owned = cycles // groups
    step = owned // PARTS
    window = step * cap
    tblk = groups * sub
    starts = (jnp.cumsum(cycle_sizes) - cycle_sizes).astype(jnp.int32)
    me = lax.axis_index("pix")
    slots = jnp.arange(cap, dtype=jnp.int32)

    order = jnp.pad(pixel_order, (0, window))
    series = block.T

    outs = []
    for part in range(PARTS):
        wanted = jnp.stack(
            [
                lax.dynamic_slice_in_dim(order, starts[d * owned + part * step], window, 0)
                for d in range(groups)
            ]
        )
        chunks = jnp.take(series, wanted, axis=0)
        got = lax.all_to_all(chunks, "pix", 0, 0, tiled=True)
        got = jnp.pad(got, ((0, 0), (0, cap), (0, 0)))
        first = me * owned + part * step
        picked = []
        for l in range(step):
            rows = lax.dynamic_slice_in_dim(got, starts[first + l] - starts[first], cap, 1)
            picked.append(jnp.where((slots < cycle_sizes[first + l])[None, :, None], rows, 0.0))
        picked = jnp.stack(picked)
        picked = jnp.transpose(picked, (0, 2, 1, 3)).reshape(step, cap, tblk)

        total = jnp.sum(picked, axis=1, keepdims=True)
        rimmed = halo_frames(picked / total, REACH)
        smooth = kernel[0] * rimmed[..., 0:tblk]
        for shift_step in range(1, 2 * REACH + 1):
            smooth = smooth + kernel[shift_step] * rimmed[..., shift_step : shift_step + tblk]
        smooth = jnp.swapaxes(smooth, 1, 2)

        scale = lax.dynamic_slice_in_dim(cycle_sizes, first, step).astype(jnp.float32)
        right = lax.all_gather(smooth, "tm", axis=1, tiled=True)
        outs.append(correlate(smooth * scale[:, None, None], right))
    return jnp.concatenate(outs, 0)


def solution(mesh):
    placed = (P("tm", "pix", None), P(), P(), P())
    return jax.shard_map(
        per_device, mesh=mesh, in_specs=placed, out_specs=P("pix", "tm", None), check_vma=False
    )
```

```python
import jax
import jax.numpy as jnp
from jax import lax
from jax.sharding import PartitionSpec as P

REACH = 2
PARTS = 4


def halo_frames(block, width):
    count = lax.axis_size("tm")
    forward = [(i, i + 1) for i in range(count - 1)]
    backward = [(i + 1, i) for i in range(count - 1)]
    n = block.shape[-1]
    low = lax.ppermute(block[..., n - width :], "tm", forward)
    high = lax.ppermute(block[..., :width], "tm", backward)
    return jnp.concatenate([low, block, high], axis=-1)


def correlate(left, right):
    return jnp.einsum(
        "rfs,rgs->rfg", left, right, precision=lax.Precision.HIGH, preferred_element_type=jnp.float32
    )


def per_device(frames, pixel_order, cycle_sizes, kernel):
    block = frames[0]
    sub, pixels = block.shape
    cycles = cycle_sizes.shape[0]
    cap = 2 * pixels // cycles
    groups = lax.axis_size("pix")
    owned = cycles // groups
    step = owned // PARTS
    window = step * cap
    tblk = groups * sub
    starts = (jnp.cumsum(cycle_sizes) - cycle_sizes).astype(jnp.int32).reshape(groups, owned)
    sends = starts[:, ::step]
    me = lax.axis_index("pix")
    mine = lax.dynamic_index_in_dim(starts, me, 0, keepdims=False)
    sizes = lax.dynamic_index_in_dim(cycle_sizes.reshape(groups, owned), me, 0, keepdims=False)
    slots = jnp.arange(cap, dtype=jnp.int32)

    order = jnp.pad(pixel_order, (0, window))
    series = block.T

    outs = []
    for part in range(PARTS):
        wanted = jnp.stack(
            [lax.dynamic_slice_in_dim(order, sends[d, part], window, 0) for d in range(groups)]
        )
        chunks = jnp.take(series, wanted, axis=0)
        got = lax.all_to_all(chunks, "pix", 0, 0, tiled=True)
        got = jnp.pad(got, ((0, 0), (0, cap), (0, 0)))
        first = part * step
        offsets = mine[first : first + step] - mine[first]
        masks = slots[None, :] < sizes[first : first + step, None]
        picked = []
        for l in range(step):
            rows = lax.dynamic_slice_in_dim(got, offsets[l], cap, 1)
            picked.append(jnp.where(masks[l][None, :, None], rows, 0.0))
        picked = jnp.stack(picked)
        picked = jnp.transpose(picked, (0, 2, 1, 3)).reshape(step, cap, tblk)

        total = jnp.sum(picked, axis=1, keepdims=True)
        rimmed = halo_frames(picked / total, REACH)
        smooth = kernel[0] * rimmed[..., 0:tblk]
        for shift_step in range(1, 2 * REACH + 1):
            smooth = smooth + kernel[shift_step] * rimmed[..., shift_step : shift_step + tblk]
        smooth = jnp.swapaxes(smooth, 1, 2)

        scale = sizes[first : first + step].astype(jnp.float32)
        right = lax.all_gather(smooth, "tm", axis=1, tiled=True)
        outs.append(correlate(smooth * scale[:, None, None], right))
    return jnp.concatenate(outs, 0)


def solution(mesh):
    placed = (P("tm", "pix", None), P(), P(), P())
    return jax.shard_map(
        per_device, mesh=mesh, in_specs=placed, out_specs=P("pix", "tm", None), check_vma=False
    )
```

```python
import jax
import jax.numpy as jnp
from jax import lax
from jax.sharding import PartitionSpec as P

REACH = 2
PARTS = 4


def halo_frames(block, width):
    count = lax.axis_size("tm")
    forward = [(i, i + 1) for i in range(count - 1)]
    backward = [(i + 1, i) for i in range(count - 1)]
    n = block.shape[-1]
    low = lax.ppermute(block[..., n - width :], "tm", forward)
    high = lax.ppermute(block[..., :width], "tm", backward)
    return jnp.concatenate([low, block, high], axis=-1)


def correlate(left, right):
    return jnp.einsum(
        "rfs,rgs->rfg", left, right, precision=lax.Precision.HIGH, preferred_element_type=jnp.float32
    )


def per_device(frames, pixel_order, cycle_sizes, kernel):
    block = frames[0]
    sub, pixels = block.shape
    cycles = cycle_sizes.shape[0]
    cap = 2 * pixels // cycles
    groups = lax.axis_size("pix")
    owned = cycles // groups
    step = owned // PARTS
    window = step * cap
    tblk = groups * sub
    starts = (jnp.cumsum(cycle_sizes) - cycle_sizes).astype(jnp.int32).reshape(groups, owned)
    sends = starts[:, ::step]
    me = lax.axis_index("pix")
    mine = lax.dynamic_index_in_dim(starts, me, 0, keepdims=False)
    sizes = lax.dynamic_index_in_dim(cycle_sizes.reshape(groups, owned), me, 0, keepdims=False)
    slots = jnp.arange(cap, dtype=jnp.int32)

    lanes = 128
    span = window + lanes
    order = jnp.pad(pixel_order, (0, span)).reshape(-1, lanes)
    aligned = (sends // lanes) * lanes
    series = block.T
    reach = jnp.arange(span, dtype=jnp.int32)

    outs = []
    for part in range(PARTS):
        rows = (aligned[:, part] // lanes)[:, None] + jnp.arange(span // lanes, dtype=jnp.int32)
        wanted = jnp.take(order, rows, axis=0).reshape(groups * span)
        chunks = jnp.take(series, wanted, axis=0).reshape(groups, span, sub)
        got = lax.all_to_all(chunks, "pix", 0, 0, tiled=True)

        first = part * step
        offsets = mine[first : first + step] - (mine[first] // lanes) * lanes
        hit = reach[None, None, :] == offsets[:, None, None] + slots[None, :, None]
        hit = hit & (slots[None, :, None] < sizes[first : first + step, None, None])
        picked = jnp.einsum(
            "lcj,sjf->lcsf",
            hit.astype(jnp.float32),
            got,
            precision=lax.Precision.HIGHEST,
            preferred_element_type=jnp.float32,
        ).reshape(step, cap, tblk)

        total = jnp.sum(picked, axis=1, keepdims=True)
        rimmed = halo_frames(picked / total, REACH)
        smooth = kernel[0] * rimmed[..., 0:tblk]
        for shift_step in range(1, 2 * REACH + 1):
            smooth = smooth + kernel[shift_step] * rimmed[..., shift_step : shift_step + tblk]
        smooth = jnp.swapaxes(smooth, 1, 2)

        scale = sizes[first : first + step].astype(jnp.float32)
        right = lax.all_gather(smooth, "tm", axis=1, tiled=True)
        outs.append(correlate(smooth * scale[:, None, None], right))
    return jnp.concatenate(outs, 0)


def solution(mesh):
    placed = (P("tm", "pix", None), P(), P(), P())
    return jax.shard_map(
        per_device, mesh=mesh, in_specs=placed, out_specs=P("pix", "tm", None), check_vma=False
    )
```

```python
import jax
import jax.numpy as jnp
from jax import lax
from jax.sharding import PartitionSpec as P

REACH = 2
PARTS = 2


def halo_frames(block, width):
    count = lax.axis_size("tm")
    forward = [(i, i + 1) for i in range(count - 1)]
    backward = [(i + 1, i) for i in range(count - 1)]
    n = block.shape[-1]
    low = lax.ppermute(block[..., n - width :], "tm", forward)
    high = lax.ppermute(block[..., :width], "tm", backward)
    return jnp.concatenate([low, block, high], axis=-1)


def correlate(left, right):
    return jnp.einsum(
        "rfs,rgs->rfg", left, right, precision=lax.Precision.HIGH, preferred_element_type=jnp.float32
    )


def per_device(frames, pixel_order, cycle_sizes, kernel):
    block = frames[0]
    sub, pixels = block.shape
    cycles = cycle_sizes.shape[0]
    cap = 2 * pixels // cycles
    groups = lax.axis_size("pix")
    owned = cycles // groups
    step = owned // PARTS
    window = step * cap
    tblk = groups * sub
    starts = (jnp.cumsum(cycle_sizes) - cycle_sizes).astype(jnp.int32).reshape(groups, owned)
    sends = starts[:, ::step]
    me = lax.axis_index("pix")
    mine = lax.dynamic_index_in_dim(starts, me, 0, keepdims=False)
    sizes = lax.dynamic_index_in_dim(cycle_sizes.reshape(groups, owned), me, 0, keepdims=False)
    slots = jnp.arange(cap, dtype=jnp.int32)

    order = jnp.pad(pixel_order, (0, window))
    series = block.T

    outs = []
    for part in range(PARTS):
        wanted = jnp.stack(
            [lax.dynamic_slice_in_dim(order, sends[d, part], window, 0) for d in range(groups)]
        )
        chunks = jnp.take(series, wanted, axis=0)
        got = lax.all_to_all(chunks, "pix", 0, 0, tiled=True)
        got = jnp.pad(got, ((0, 0), (0, cap), (0, 0)))
        first = part * step
        offsets = mine[first : first + step] - mine[first]
        masks = slots[None, :] < sizes[first : first + step, None]
        picked = []
        for l in range(step):
            rows = lax.dynamic_slice_in_dim(got, offsets[l], cap, 1)
            picked.append(jnp.where(masks[l][None, :, None], rows, 0.0))
        picked = jnp.stack(picked)
        picked = jnp.transpose(picked, (0, 2, 1, 3)).reshape(step, cap, tblk)

        total = jnp.sum(picked, axis=1, keepdims=True)
        rimmed = halo_frames(picked / total, REACH)
        smooth = kernel[0] * rimmed[..., 0:tblk]
        for shift_step in range(1, 2 * REACH + 1):
            smooth = smooth + kernel[shift_step] * rimmed[..., shift_step : shift_step + tblk]
        smooth = jnp.swapaxes(smooth, 1, 2)

        scale = sizes[first : first + step].astype(jnp.float32)
        right = lax.all_gather(smooth, "tm", axis=1, tiled=True)
        outs.append(correlate(smooth * scale[:, None, None], right))
    return jnp.concatenate(outs, 0)


def solution(mesh):
    placed = (P("tm", "pix", None), P(), P(), P())
    return jax.shard_map(
        per_device, mesh=mesh, in_specs=placed, out_specs=P("pix", "tm", None), check_vma=False
    )
```

```python
import jax
import jax.numpy as jnp
from jax import lax
from jax.sharding import PartitionSpec as P

REACH = 2
PARTS = 2


def halo_frames(block, width):
    count = lax.axis_size("tm")
    forward = [(i, i + 1) for i in range(count - 1)]
    backward = [(i + 1, i) for i in range(count - 1)]
    n = block.shape[-1]
    low = lax.ppermute(block[..., n - width :], "tm", forward)
    high = lax.ppermute(block[..., :width], "tm", backward)
    return jnp.concatenate([low, block, high], axis=-1)


def correlate(left, right):
    return jnp.einsum(
        "rfs,rgs->rfg", left, right, precision=lax.Precision.HIGH, preferred_element_type=jnp.float32
    )


def per_device(frames, pixel_order, cycle_sizes, kernel):
    block = frames[0]
    sub, pixels = block.shape
    cycles = cycle_sizes.shape[0]
    cap = 2 * pixels // cycles
    groups = lax.axis_size("pix")
    owned = cycles // groups
    step = owned // PARTS
    window = step * cap
    tblk = groups * sub
    starts = (jnp.cumsum(cycle_sizes) - cycle_sizes).astype(jnp.int32).reshape(groups, owned)
    sends = starts[:, ::step]
    me = lax.axis_index("pix")
    mine = lax.dynamic_index_in_dim(starts, me, 0, keepdims=False)
    sizes = lax.dynamic_index_in_dim(cycle_sizes.reshape(groups, owned), me, 0, keepdims=False)
    slots = jnp.arange(cap, dtype=jnp.int32)

    order = jnp.pad(pixel_order, (0, window))
    series = block.T

    outs = []
    for part in range(PARTS):
        wanted = jnp.stack(
            [lax.dynamic_slice_in_dim(order, sends[d, part], window, 0) for d in range(groups)]
        )
        chunks = jnp.take(series, wanted, axis=0)
        got = lax.all_to_all(chunks, "pix", 0, 0, tiled=True)
        got = jnp.pad(got, ((0, 0), (0, cap), (0, 0)))
        first = part * step
        offsets = mine[first : first + step] - mine[first]
        masks = slots[None, :] < sizes[first : first + step, None]
        picked = []
        for l in range(step):
            rows = lax.dynamic_slice_in_dim(got, offsets[l], cap, 1)
            picked.append(jnp.where(masks[l][None, :, None], rows, 0.0))
        picked = jnp.stack(picked)
        picked = jnp.transpose(picked, (0, 2, 1, 3)).reshape(step, cap, tblk)

        total = jnp.sum(picked, axis=1, keepdims=True)
        rimmed = halo_frames(picked / total, REACH)
        smooth = kernel[0] * rimmed[..., 0:tblk]
        for shift_step in range(1, 2 * REACH + 1):
            smooth = smooth + kernel[shift_step] * rimmed[..., shift_step : shift_step + tblk]
        smooth = jnp.swapaxes(smooth, 1, 2)

        scale = sizes[first : first + step].astype(jnp.float32)
        right = lax.all_gather(smooth, "tm", axis=1, tiled=True)
        outs.append(correlate(smooth * scale[:, None, None], right))
    result = lax.optimization_barrier(jnp.pad(jnp.concatenate(outs[:-1], 0), ((0, step), (0, 0), (0, 0))))
    return lax.dynamic_update_slice_in_dim(result, outs[-1], owned - step, 0)


def solution(mesh):
    placed = (P("tm", "pix", None), P(), P(), P())
    return jax.shard_map(
        per_device, mesh=mesh, in_specs=placed, out_specs=P("pix", "tm", None), check_vma=False
    )
```

```python
import jax
import jax.numpy as jnp
from jax import lax
from jax.sharding import PartitionSpec as P

REACH = 2
PARTS = 2


def halo_frames(block, width):
    count = lax.axis_size("tm")
    forward = [(i, i + 1) for i in range(count - 1)]
    backward = [(i + 1, i) for i in range(count - 1)]
    n = block.shape[-1]
    low = lax.ppermute(block[..., n - width :], "tm", forward)
    high = lax.ppermute(block[..., :width], "tm", backward)
    return jnp.concatenate([low, block, high], axis=-1)


def correlate(left, right):
    return jnp.einsum(
        "rfs,rgs->rfg", left, right, precision=lax.Precision.HIGH, preferred_element_type=jnp.float32
    )


def per_device(frames, pixel_order, cycle_sizes, kernel):
    block = frames[0]
    sub, pixels = block.shape
    cycles = cycle_sizes.shape[0]
    cap = 2 * pixels // cycles
    groups = lax.axis_size("pix")
    owned = cycles // groups
    step = owned // PARTS
    window = step * cap
    tblk = groups * sub
    starts = (jnp.cumsum(cycle_sizes) - cycle_sizes).astype(jnp.int32).reshape(groups, owned)
    sends = starts[:, ::step]
    me = lax.axis_index("pix")
    mine = lax.dynamic_index_in_dim(starts, me, 0, keepdims=False)
    sizes = lax.dynamic_index_in_dim(cycle_sizes.reshape(groups, owned), me, 0, keepdims=False)
    slots = jnp.arange(cap, dtype=jnp.int32)

    lanes = 128
    span = window + lanes
    count = pixels // lanes + span // lanes
    order = jnp.pad(pixel_order, (0, count * lanes - pixels)).reshape(count, lanes).astype(jnp.float32)
    aligned = (sends // lanes) * lanes
    rows = (aligned // lanes)[:, :, None] + jnp.arange(span // lanes, dtype=jnp.int32)
    pick_rows = (rows[..., None] == jnp.arange(count, dtype=jnp.int32)).astype(jnp.float32)
    windows = jnp.einsum(
        "dprk,kl->pdrl", pick_rows, order, precision=lax.Precision.HIGHEST, preferred_element_type=jnp.float32
    )
    windows = windows.astype(jnp.int32).reshape(PARTS, groups * span)
    series = block.T

    outs = []
    for part in range(PARTS):
        chunks = jnp.take(series, windows[part], axis=0).reshape(groups, span, sub)
        got = lax.all_to_all(chunks, "pix", 0, 0, tiled=True)
        got = jnp.pad(got, ((0, 0), (0, cap), (0, 0)))
        first = part * step
        offsets = mine[first : first + step] - (mine[first] // lanes) * lanes
        masks = slots[None, :] < sizes[first : first + step, None]
        picked = []
        for l in range(step):
            rows = lax.dynamic_slice_in_dim(got, offsets[l], cap, 1)
            picked.append(jnp.where(masks[l][None, :, None], rows, 0.0))
        picked = jnp.stack(picked)
        picked = jnp.transpose(picked, (0, 2, 1, 3)).reshape(step, cap, tblk)

        total = jnp.sum(picked, axis=1, keepdims=True)
        rimmed = halo_frames(picked / total, REACH)
        smooth = kernel[0] * rimmed[..., 0:tblk]
        for shift_step in range(1, 2 * REACH + 1):
            smooth = smooth + kernel[shift_step] * rimmed[..., shift_step : shift_step + tblk]
        smooth = jnp.swapaxes(smooth, 1, 2)

        scale = sizes[first : first + step].astype(jnp.float32)
        right = lax.all_gather(smooth, "tm", axis=1, tiled=True)
        outs.append(correlate(smooth * scale[:, None, None], right))
    result = lax.optimization_barrier(jnp.pad(jnp.concatenate(outs[:-1], 0), ((0, step), (0, 0), (0, 0))))
    return lax.dynamic_update_slice_in_dim(result, outs[-1], owned - step, 0)


def solution(mesh):
    placed = (P("tm", "pix", None), P(), P(), P())
    return jax.shard_map(
        per_device, mesh=mesh, in_specs=placed, out_specs=P("pix", "tm", None), check_vma=False
    )
```

```python
import jax
import jax.numpy as jnp
from jax import lax
from jax.sharding import PartitionSpec as P

REACH = 2
PARTS = 2


def halo_frames(block, width):
    count = lax.axis_size("tm")
    forward = [(i, i + 1) for i in range(count - 1)]
    backward = [(i + 1, i) for i in range(count - 1)]
    n = block.shape[-1]
    low = lax.ppermute(block[..., n - width :], "tm", forward)
    high = lax.ppermute(block[..., :width], "tm", backward)
    return jnp.concatenate([low, block, high], axis=-1)


def correlate(left, right):
    return jnp.einsum(
        "rfs,rgs->rfg", left, right, precision=lax.Precision.HIGH, preferred_element_type=jnp.float32
    )


def per_device(frames, pixel_order, cycle_sizes, kernel):
    block = frames[0]
    sub, pixels = block.shape
    cycles = cycle_sizes.shape[0]
    cap = 2 * pixels // cycles
    groups = lax.axis_size("pix")
    owned = cycles // groups
    step = owned // PARTS
    window = step * cap
    tblk = groups * sub
    starts = (jnp.cumsum(cycle_sizes) - cycle_sizes).astype(jnp.int32).reshape(groups, owned)
    sends = starts[:, ::step]
    me = lax.axis_index("pix")
    mine = lax.dynamic_index_in_dim(starts, me, 0, keepdims=False)
    sizes = lax.dynamic_index_in_dim(cycle_sizes.reshape(groups, owned), me, 0, keepdims=False)
    slots = jnp.arange(cap, dtype=jnp.int32)

    lanes = 128
    span = window + lanes
    count = pixels // lanes + span // lanes
    order = jnp.pad(pixel_order, (0, count * lanes - pixels)).reshape(count, lanes).astype(jnp.float32)
    aligned = (sends // lanes) * lanes
    rows = (aligned // lanes)[:, :, None] + jnp.arange(span // lanes, dtype=jnp.int32)
    pick_rows = (rows[..., None] == jnp.arange(count, dtype=jnp.int32)).astype(jnp.float32)
    windows = jnp.einsum(
        "dprk,kl->pdrl", pick_rows, order, precision=lax.Precision.HIGHEST, preferred_element_type=jnp.float32
    )
    windows = windows.astype(jnp.int32).reshape(PARTS, groups * span)
    series = block.T

    outs = []
    for part in range(PARTS):
        chunks = series.at[windows[part]].get(mode="promise_in_bounds").reshape(groups, span, sub)
        got = lax.all_to_all(chunks, "pix", 0, 0, tiled=True)
        got = jnp.pad(got, ((0, 0), (0, cap), (0, 0)))
        first = part * step
        offsets = mine[first : first + step] - (mine[first] // lanes) * lanes
        masks = slots[None, :] < sizes[first : first + step, None]
        picked = []
        for l in range(step):
            rows = lax.dynamic_slice_in_dim(got, offsets[l], cap, 1)
            picked.append(jnp.where(masks[l][None, :, None], rows, 0.0))
        picked = jnp.stack(picked)
        picked = jnp.transpose(picked, (0, 2, 1, 3)).reshape(step, cap, tblk)

        total = jnp.sum(picked, axis=1, keepdims=True)
        rimmed = halo_frames(picked / total, REACH)
        smooth = kernel[0] * rimmed[..., 0:tblk]
        for shift_step in range(1, 2 * REACH + 1):
            smooth = smooth + kernel[shift_step] * rimmed[..., shift_step : shift_step + tblk]
        smooth = jnp.swapaxes(smooth, 1, 2)

        scale = sizes[first : first + step].astype(jnp.float32)
        right = lax.all_gather(smooth, "tm", axis=1, tiled=True)
        outs.append(correlate(smooth * scale[:, None, None], right))
    result = lax.optimization_barrier(jnp.pad(jnp.concatenate(outs[:-1], 0), ((0, step), (0, 0), (0, 0))))
    return lax.dynamic_update_slice_in_dim(result, outs[-1], owned - step, 0)


def solution(mesh):
    placed = (P("tm", "pix", None), P(), P(), P())
    return jax.shard_map(
        per_device, mesh=mesh, in_specs=placed, out_specs=P("pix", "tm", None), check_vma=False
    )
```

```python
import jax
import jax.numpy as jnp
from jax import lax
from jax.sharding import PartitionSpec as P

REACH = 2
PARTS = 2


def halo_frames(block, width):
    count = lax.axis_size("tm")
    forward = [(i, i + 1) for i in range(count - 1)]
    backward = [(i + 1, i) for i in range(count - 1)]
    n = block.shape[-1]
    low = lax.ppermute(block[..., n - width :], "tm", forward)
    high = lax.ppermute(block[..., :width], "tm", backward)
    return jnp.concatenate([low, block, high], axis=-1)


def correlate(left, right):
    return jnp.einsum(
        "rfs,rgs->rfg", left, right, precision=lax.Precision.HIGH, preferred_element_type=jnp.float32
    )


def per_device(frames, pixel_order, cycle_sizes, kernel):
    block = frames[0]
    sub, pixels = block.shape
    cycles = cycle_sizes.shape[0]
    cap = 2 * pixels // cycles
    groups = lax.axis_size("pix")
    owned = cycles // groups
    step = owned // PARTS
    window = step * cap
    tblk = groups * sub
    starts = (jnp.cumsum(cycle_sizes) - cycle_sizes).astype(jnp.int32).reshape(groups, owned)
    sends = starts[:, ::step]
    me = lax.axis_index("pix")
    mine = lax.dynamic_index_in_dim(starts, me, 0, keepdims=False)
    sizes = lax.dynamic_index_in_dim(cycle_sizes.reshape(groups, owned), me, 0, keepdims=False)
    slots = jnp.arange(cap, dtype=jnp.int32)

    lanes = 128
    span = window + lanes
    count = pixels // lanes + span // lanes
    order = jnp.pad(pixel_order, (0, count * lanes - pixels)).reshape(count, lanes).astype(jnp.float32)
    aligned = (sends // lanes) * lanes
    rows = (aligned // lanes)[:, :, None] + jnp.arange(span // lanes, dtype=jnp.int32)
    pick_rows = (rows[..., None] == jnp.arange(count, dtype=jnp.int32)).astype(jnp.float32)
    windows = jnp.einsum(
        "dprk,kl->pdrl", pick_rows, order, precision=lax.Precision.HIGHEST, preferred_element_type=jnp.float32
    )
    windows = windows.astype(jnp.int32).reshape(PARTS, groups * span)
    series = block.T

    outs = []
    for part in range(PARTS):
        chunks = series.at[windows[part]].get(mode="promise_in_bounds").reshape(groups, span, sub)
        got = lax.all_to_all(chunks, "pix", 0, 0, tiled=True)
        got = jnp.pad(got, ((0, 0), (0, cap), (0, 0)))
        first = part * step
        offsets = mine[first : first + step] - (mine[first] // lanes) * lanes
        masks = slots[None, :] < sizes[first : first + step, None]
        picked = []
        for l in range(step):
            rows = lax.dynamic_slice_in_dim(got, offsets[l], cap, 1)
            picked.append(jnp.where(masks[l][None, :, None], rows, 0.0))
        picked = jnp.stack(picked)
        picked = jnp.transpose(picked, (0, 2, 1, 3)).reshape(step, cap, tblk)

        total = jnp.sum(picked, axis=1, keepdims=True)
        scaled = picked / total
        scale = sizes[first : first + step].astype(jnp.float32)[:, None, None]
        if part == 0:
            whole = lax.all_gather(jnp.swapaxes(scaled, 1, 2), "tm", axis=1, tiled=True)
            frames_all = whole.shape[1]
            rimmed = jnp.pad(whole, ((0, 0), (REACH, REACH), (0, 0)))
            right = kernel[0] * rimmed[:, 0:frames_all]
            for shift_step in range(1, 2 * REACH + 1):
                right = right + kernel[shift_step] * rimmed[:, shift_step : shift_step + frames_all]
            smooth = lax.dynamic_slice_in_dim(right, lax.axis_index("tm") * tblk, tblk, 1)
        else:
            rimmed = halo_frames(scaled, REACH)
            smooth = kernel[0] * rimmed[..., 0:tblk]
            for shift_step in range(1, 2 * REACH + 1):
                smooth = smooth + kernel[shift_step] * rimmed[..., shift_step : shift_step + tblk]
            smooth = jnp.swapaxes(smooth, 1, 2)
            right = lax.all_gather(smooth, "tm", axis=1, tiled=True)
        outs.append(correlate(smooth * scale, right))
    result = lax.optimization_barrier(jnp.pad(jnp.concatenate(outs[:-1], 0), ((0, step), (0, 0), (0, 0))))
    return lax.dynamic_update_slice_in_dim(result, outs[-1], owned - step, 0)


def solution(mesh):
    placed = (P("tm", "pix", None), P(), P(), P())
    return jax.shard_map(
        per_device, mesh=mesh, in_specs=placed, out_specs=P("pix", "tm", None), check_vma=False
    )
```

```python
import jax
import jax.numpy as jnp
from jax import lax
from jax.sharding import PartitionSpec as P

REACH = 2
PARTS = 2


def halo_frames(block, width):
    count = lax.axis_size("tm")
    forward = [(i, i + 1) for i in range(count - 1)]
    backward = [(i + 1, i) for i in range(count - 1)]
    n = block.shape[-1]
    low = lax.ppermute(block[..., n - width :], "tm", forward)
    high = lax.ppermute(block[..., :width], "tm", backward)
    return jnp.concatenate([low, block, high], axis=-1)


def correlate(left, right):
    return jnp.einsum(
        "rfs,rgs->rfg", left, right, precision=lax.Precision.HIGH, preferred_element_type=jnp.float32
    )


def per_device(frames, pixel_order, cycle_sizes, kernel):
    block = frames[0]
    sub, pixels = block.shape
    cycles = cycle_sizes.shape[0]
    cap = 2 * pixels // cycles
    groups = lax.axis_size("pix")
    owned = cycles // groups
    step = owned // PARTS
    window = step * cap
    tblk = groups * sub
    starts = (jnp.cumsum(cycle_sizes) - cycle_sizes).astype(jnp.int32).reshape(groups, owned)
    sends = starts[:, ::step]
    me = lax.axis_index("pix")
    mine = lax.dynamic_index_in_dim(starts, me, 0, keepdims=False)
    sizes = lax.dynamic_index_in_dim(cycle_sizes.reshape(groups, owned), me, 0, keepdims=False)
    slots = jnp.arange(cap, dtype=jnp.int32)

    lanes = 32
    span = window + lanes
    count = pixels // lanes + span // lanes
    order = jnp.pad(pixel_order, (0, count * lanes - pixels)).reshape(count, lanes).astype(jnp.float32)
    aligned = (sends // lanes) * lanes
    rows = (aligned // lanes)[:, :, None] + jnp.arange(span // lanes, dtype=jnp.int32)
    pick_rows = (rows[..., None] == jnp.arange(count, dtype=jnp.int32)).astype(jnp.float32)
    windows = jnp.einsum(
        "dprk,kl->pdrl", pick_rows, order, precision=lax.Precision.HIGHEST, preferred_element_type=jnp.float32
    )
    windows = windows.astype(jnp.int32).reshape(PARTS, groups * span)
    series = block.T

    outs = []
    for part in range(PARTS):
        chunks = series.at[windows[part]].get(mode="promise_in_bounds").reshape(groups, span, sub)
        got = lax.all_to_all(chunks, "pix", 0, 0, tiled=True)
        got = jnp.pad(got, ((0, 0), (0, cap), (0, 0)))
        first = part * step
        offsets = mine[first : first + step] - (mine[first] // lanes) * lanes
        masks = slots[None, :] < sizes[first : first + step, None]
        picked = []
        for l in range(step):
            rows = lax.dynamic_slice_in_dim(got, offsets[l], cap, 1)
            picked.append(jnp.where(masks[l][None, :, None], rows, 0.0))
        picked = jnp.stack(picked)
        picked = jnp.transpose(picked, (0, 2, 1, 3)).reshape(step, cap, tblk)

        total = jnp.sum(picked, axis=1, keepdims=True)
        scaled = picked / total
        scale = sizes[first : first + step].astype(jnp.float32)[:, None, None]
        if part == 0:
            whole = lax.all_gather(jnp.swapaxes(scaled, 1, 2), "tm", axis=1, tiled=True)
            frames_all = whole.shape[1]
            rimmed = jnp.pad(whole, ((0, 0), (REACH, REACH), (0, 0)))
            right = kernel[0] * rimmed[:, 0:frames_all]
            for shift_step in range(1, 2 * REACH + 1):
                right = right + kernel[shift_step] * rimmed[:, shift_step : shift_step + frames_all]
            smooth = lax.dynamic_slice_in_dim(right, lax.axis_index("tm") * tblk, tblk, 1)
        else:
            rimmed = halo_frames(scaled, REACH)
            smooth = kernel[0] * rimmed[..., 0:tblk]
            for shift_step in range(1, 2 * REACH + 1):
                smooth = smooth + kernel[shift_step] * rimmed[..., shift_step : shift_step + tblk]
            smooth = jnp.swapaxes(smooth, 1, 2)
            right = lax.all_gather(smooth, "tm", axis=1, tiled=True)
        outs.append(correlate(smooth * scale, right))
    result = lax.optimization_barrier(jnp.pad(jnp.concatenate(outs[:-1], 0), ((0, step), (0, 0), (0, 0))))
    return lax.dynamic_update_slice_in_dim(result, outs[-1], owned - step, 0)


def solution(mesh):
    placed = (P("tm", "pix", None), P(), P(), P())
    return jax.shard_map(
        per_device, mesh=mesh, in_specs=placed, out_specs=P("pix", "tm", None), check_vma=False
    )
```

```python
import jax
import jax.numpy as jnp
from jax import lax
from jax.sharding import PartitionSpec as P

REACH = 2


def halo_frames(block, width):
    count = lax.axis_size("tm")
    forward = [(i, i + 1) for i in range(count - 1)]
    backward = [(i + 1, i) for i in range(count - 1)]
    n = block.shape[-1]
    low = lax.ppermute(block[..., n - width :], "tm", forward)
    high = lax.ppermute(block[..., :width], "tm", backward)
    return jnp.concatenate([low, block, high], axis=-1)


def correlate(left, right):
    return jnp.einsum(
        "rfs,rgs->rfg", left, right, precision=lax.Precision.HIGH, preferred_element_type=jnp.float32
    )


def per_device(frames, pixel_order, cycle_sizes, kernel):
    block = frames[0]
    sub, pixels = block.shape
    cycles = cycle_sizes.shape[0]
    cap = 2 * pixels // cycles
    groups = lax.axis_size("pix")
    owned = cycles // groups
    counts = [owned - owned * 5 // 8, owned * 5 // 8]
    firsts = [sum(counts[:i]) for i in range(len(counts))]
    tblk = groups * sub
    starts = (jnp.cumsum(cycle_sizes) - cycle_sizes).astype(jnp.int32).reshape(groups, owned)
    me = lax.axis_index("pix")
    mine = lax.dynamic_index_in_dim(starts, me, 0, keepdims=False)
    sizes = lax.dynamic_index_in_dim(cycle_sizes.reshape(groups, owned), me, 0, keepdims=False)
    slots = jnp.arange(cap, dtype=jnp.int32)

    lanes = 32
    longest = max(counts) * cap + lanes
    count = pixels // lanes + longest // lanes
    order = jnp.pad(pixel_order, (0, count * lanes - pixels)).reshape(count, lanes).astype(jnp.float32)
    series = block.T

    outs = []
    for part, (step, first) in enumerate(zip(counts, firsts)):
        span = step * cap + lanes
        aligned = (starts[:, first] // lanes) * lanes
        rows = (aligned // lanes)[:, None] + jnp.arange(span // lanes, dtype=jnp.int32)
        pick_rows = (rows[..., None] == jnp.arange(count, dtype=jnp.int32)).astype(jnp.float32)
        window = jnp.einsum(
            "drk,kl->drl", pick_rows, order, precision=lax.Precision.HIGHEST, preferred_element_type=jnp.float32
        )
        window = window.astype(jnp.int32).reshape(groups * span)
        chunks = series.at[window].get(mode="promise_in_bounds").reshape(groups, span, sub)
        got = lax.all_to_all(chunks, "pix", 0, 0, tiled=True)
        got = jnp.pad(got, ((0, 0), (0, cap), (0, 0)))
        offsets = mine[first : first + step] - (mine[first] // lanes) * lanes
        masks = slots[None, :] < sizes[first : first + step, None]
        picked = []
        for l in range(step):
            taken = lax.dynamic_slice_in_dim(got, offsets[l], cap, 1)
            picked.append(jnp.where(masks[l][None, :, None], taken, 0.0))
        picked = jnp.stack(picked)
        picked = jnp.transpose(picked, (0, 2, 1, 3)).reshape(step, cap, tblk)

        total = jnp.sum(picked, axis=1, keepdims=True)
        scaled = picked / total
        scale = sizes[first : first + step].astype(jnp.float32)[:, None, None]
        if part == 0:
            whole = lax.all_gather(jnp.swapaxes(scaled, 1, 2), "tm", axis=1, tiled=True)
            frames_all = whole.shape[1]
            rimmed = jnp.pad(whole, ((0, 0), (REACH, REACH), (0, 0)))
            right = kernel[0] * rimmed[:, 0:frames_all]
            for shift_step in range(1, 2 * REACH + 1):
                right = right + kernel[shift_step] * rimmed[:, shift_step : shift_step + frames_all]
            smooth = lax.dynamic_slice_in_dim(right, lax.axis_index("tm") * tblk, tblk, 1)
        else:
            rimmed = halo_frames(scaled, REACH)
            smooth = kernel[0] * rimmed[..., 0:tblk]
            for shift_step in range(1, 2 * REACH + 1):
                smooth = smooth + kernel[shift_step] * rimmed[..., shift_step : shift_step + tblk]
            smooth = jnp.swapaxes(smooth, 1, 2)
            right = lax.all_gather(smooth, "tm", axis=1, tiled=True)
        outs.append(correlate(smooth * scale, right))
    last = counts[-1]
    result = lax.optimization_barrier(jnp.pad(jnp.concatenate(outs[:-1], 0), ((0, last), (0, 0), (0, 0))))
    return lax.dynamic_update_slice_in_dim(result, outs[-1], owned - last, 0)


def solution(mesh):
    placed = (P("tm", "pix", None), P(), P(), P())
    return jax.shard_map(
        per_device, mesh=mesh, in_specs=placed, out_specs=P("pix", "tm", None), check_vma=False
    )
```

```python
import jax
import jax.numpy as jnp
from jax import lax
from jax.sharding import PartitionSpec as P

REACH = 2


def halo_frames(block, width):
    count = lax.axis_size("tm")
    forward = [(i, i + 1) for i in range(count - 1)]
    backward = [(i + 1, i) for i in range(count - 1)]
    n = block.shape[-1]
    low = lax.ppermute(block[..., n - width :], "tm", forward)
    high = lax.ppermute(block[..., :width], "tm", backward)
    return jnp.concatenate([low, block, high], axis=-1)


def correlate(left, right):
    return jnp.einsum(
        "rfs,rgs->rfg", left, right, precision=lax.Precision.HIGH, preferred_element_type=jnp.float32
    )


def per_device(frames, pixel_order, cycle_sizes, kernel):
    block = frames[0]
    sub, pixels = block.shape
    cycles = cycle_sizes.shape[0]
    cap = 2 * pixels // cycles
    groups = lax.axis_size("pix")
    owned = cycles // groups
    counts = [owned - owned * 5 // 8, owned * 5 // 8]
    firsts = [sum(counts[:i]) for i in range(len(counts))]
    tblk = groups * sub
    starts = (jnp.cumsum(cycle_sizes) - cycle_sizes).astype(jnp.int32).reshape(groups, owned)
    me = lax.axis_index("pix")
    mine = lax.dynamic_index_in_dim(starts, me, 0, keepdims=False)
    sizes = lax.dynamic_index_in_dim(cycle_sizes.reshape(groups, owned), me, 0, keepdims=False)
    slots = jnp.arange(cap, dtype=jnp.int32)

    lanes = 16
    longest = max(counts) * cap + lanes
    count = pixels // lanes + longest // lanes
    order = jnp.pad(pixel_order, (0, count * lanes - pixels)).reshape(count, lanes).astype(jnp.float32)
    series = block.T

    outs = []
    for part, (step, first) in enumerate(zip(counts, firsts)):
        span = step * cap + lanes
        aligned = (starts[:, first] // lanes) * lanes
        rows = (aligned // lanes)[:, None] + jnp.arange(span // lanes, dtype=jnp.int32)
        pick_rows = (rows[..., None] == jnp.arange(count, dtype=jnp.int32)).astype(jnp.float32)
        window = jnp.einsum(
            "drk,kl->drl", pick_rows, order, precision=lax.Precision.HIGHEST, preferred_element_type=jnp.float32
        )
        window = window.astype(jnp.int32).reshape(groups * span)
        chunks = series.at[window].get(mode="promise_in_bounds").reshape(groups, span, sub)
        got = lax.all_to_all(chunks, "pix", 0, 0, tiled=True)
        got = jnp.pad(got, ((0, 0), (0, cap), (0, 0)))
        offsets = mine[first : first + step] - (mine[first] // lanes) * lanes
        masks = slots[None, :] < sizes[first : first + step, None]
        picked = []
        for l in range(step):
            taken = lax.dynamic_slice_in_dim(got, offsets[l], cap, 1)
            picked.append(jnp.where(masks[l][None, :, None], taken, 0.0))
        picked = jnp.stack(picked)
        picked = jnp.transpose(picked, (0, 2, 1, 3)).reshape(step, cap, tblk)

        total = jnp.sum(picked, axis=1, keepdims=True)
        scaled = picked / total
        scale = sizes[first : first + step].astype(jnp.float32)[:, None, None]
        if part == 0:
            whole = lax.all_gather(jnp.swapaxes(scaled, 1, 2), "tm", axis=1, tiled=True)
            frames_all = whole.shape[1]
            rimmed = jnp.pad(whole, ((0, 0), (REACH, REACH), (0, 0)))
            right = kernel[0] * rimmed[:, 0:frames_all]
            for shift_step in range(1, 2 * REACH + 1):
                right = right + kernel[shift_step] * rimmed[:, shift_step : shift_step + frames_all]
            smooth = lax.dynamic_slice_in_dim(right, lax.axis_index("tm") * tblk, tblk, 1)
        else:
            rimmed = halo_frames(scaled, REACH)
            smooth = kernel[0] * rimmed[..., 0:tblk]
            for shift_step in range(1, 2 * REACH + 1):
                smooth = smooth + kernel[shift_step] * rimmed[..., shift_step : shift_step + tblk]
            smooth = jnp.swapaxes(smooth, 1, 2)
            right = lax.all_gather(smooth, "tm", axis=1, tiled=True)
        outs.append(correlate(smooth * scale, right))
    last = counts[-1]
    result = lax.optimization_barrier(jnp.pad(jnp.concatenate(outs[:-1], 0), ((0, last), (0, 0), (0, 0))))
    return lax.dynamic_update_slice_in_dim(result, outs[-1], owned - last, 0)


def solution(mesh):
    placed = (P("tm", "pix", None), P(), P(), P())
    return jax.shard_map(
        per_device, mesh=mesh, in_specs=placed, out_specs=P("pix", "tm", None), check_vma=False
    )
```
